512 devices in a mesh: expert: 128 (over x, z, core), dp: 4 (over y).
Axes of the slice: x: 4, y: 4, z: 16, core: 2. Of those that a mesh axis runs over, the one named last changes fastest.
Arguments:
- tokens: bfloat16 [16384, 3584], P('expert', 'dp'), may hold values from -6 to 6
- route_ids: int32 [16384, 8], P('expert'), may hold values from 0 to 127, as said below
- gate_scores: float32 [16384, 8], P('expert'), may hold values from 0.1 to 1, as said below
- up_weight: bfloat16 [128, 3584, 1024], P('expert', 'dp'), may hold values from -0.09375 to 0.09375
- down_weight: bfloat16 [128, 1024, 3584], P('expert', None, 'dp'), may hold values from -0.1875 to 0.1875
Outputs:
- mixed: bfloat16 [16384, 3584], P('expert', 'dp')
The draws below stay inside these ranges and needn't reach their ends.
Inputs may be any that keep to these rules, and one draw needn't show every extreme that they name: `route_ids`: each row names 8 different experts. The same 2 experts are named by exactly 15 rows in every aligned block of 128 rows (the tokens of one device); in such a block every other expert is named by 8 - 1 or 8 rows. `gate_scores`: positive affinities.
All inputs are finite; a program needn't handle non-finite values.
Results may differ from the reference program's by a relative error of at most 0.017.
Values may be sent and summed in bfloat16 or wider, within the bound.
No kernel may reach another device: no remote copies, remote signals or barrier semaphores. Data moves between devices by JAX's collectives and lax.ppermute only.
A program may use at most 64 MiB of HBM per device.

```python
import jax
import jax.numpy as jnp
from jax import lax

D = 3584
HID = 1024
TOP = 8
HOT = 2
TOK_DEV = 128
EXPERTS = 128
TOKENS = 16384
HOT_MOST = 15
COLD_MOST = 8
N_EXPERT = 128
N_DP = 4


def route_table(key):
    blocks = TOKENS // TOK_DEV
    mean_rows = TOK_DEV * TOP // EXPERTS
    cold_rows = (EXPERTS - HOT) * mean_rows - HOT * (HOT_MOST - mean_rows)
    base_count = cold_rows // (EXPERTS - HOT)
    extra_count = cold_rows % (EXPERTS - HOT)
    expert_order = jax.random.permutation(jax.random.fold_in(key, 11), EXPERTS).astype(jnp.int32)

    def one_block(block_index):
        block_key = jax.random.fold_in(key, block_index)
        cold_list = jax.random.permutation(jax.random.fold_in(block_key, 1), expert_order[HOT:])
        listed = jnp.concatenate([expert_order[:HOT], cold_list]).astype(jnp.int32)
        counts = jnp.concatenate([jnp.full((HOT,), HOT_MOST, jnp.int32), jnp.where(jnp.arange(EXPERTS - HOT) < extra_count, base_count + 1, base_count).astype(jnp.int32)])
        bounds = jnp.cumsum(counts).astype(jnp.int32)
        position = jnp.arange(TOK_DEV * TOP, dtype=jnp.int32)
        owner_index = jnp.sum((position[:, None] >= bounds[None, :]).astype(jnp.int32), axis=1)
        sequence = listed[owner_index]
        layout = sequence.reshape(TOP, TOK_DEV).T
        shuffle = jax.random.permutation(jax.random.fold_in(block_key, 2), TOK_DEV)
        layout = layout[shuffle]
        sort_keys = jax.random.randint(jax.random.fold_in(block_key, 3), (TOK_DEV, TOP), 0, 1 << 20) * TOP
        sort_keys = sort_keys + jnp.arange(TOP, dtype=jnp.int32)[None, :]
        order_cols = jnp.argsort(sort_keys, axis=1)
        return jnp.take_along_axis(layout, order_cols, axis=1)
    drawn = jax.vmap(one_block)(jnp.arange(blocks, dtype=jnp.int32))
    return (drawn.reshape(TOKENS, TOP).astype(jnp.int32), expert_order[:HOT])


def draw_route_ids(key, part):
    route_rows, hot_list = route_table(key)
    return route_rows


def draw_gate_scores(key, part):
    route_rows, hot_list = route_table(key)
    hot_mask = jnp.any(route_rows[:, :, None] == hot_list[None, None, :], axis=2)
    score_key = jax.random.fold_in(key, 1000003)
    upper_key = jax.random.fold_in(score_key, 1)
    lower_key = jax.random.fold_in(score_key, 2)
    hot_values = jnp.exp(jax.random.uniform(upper_key, (TOKENS, TOP), jnp.float32, jnp.log(0.6), 0.0))
    cold_values = jnp.exp(jax.random.uniform(lower_key, (TOKENS, TOP), jnp.float32, jnp.log(0.1), jnp.log(0.4)))
    scores = jnp.where(hot_mask, hot_values, cold_values)
    return jnp.clip(scores, 0.1, 1.0).astype(jnp.float32)


def steps_of(own_key, dims, shards, smallest, top_value):
    level = 1.0
    for dim, blocks in shards:
        heights = jax.random.uniform(jax.random.fold_in(jax.random.fold_in(own_key, 6), dim), (blocks,), jnp.float32, smallest / len(shards), top_value / len(shards))
        level = level * jnp.repeat(jnp.exp(heights), dims[dim] // blocks).reshape((-1,) + (1,) * (len(dims) - 1 - dim))
    return level


def normal_values(key, extent, width, bound, shards=(), kind=jnp.bfloat16):
    entries = width * jax.random.normal(key, extent, jnp.float32)
    if shards:
        entries = entries * steps_of(key, extent, shards, -0.22, 0.18)
    return jnp.clip(entries, -bound, bound).astype(kind)


def setup_inputs(seed: int = 0) -> dict:
    arg_keys = jax.random.split(jax.random.key(seed), 6)
    tokens = normal_values(arg_keys[0], (TOKENS, D), 1.0, 6.0, ((0, 128), (1, 4)))
    route_ids = draw_route_ids(jax.random.fold_in(arg_keys[5], 71), 0)
    gate_scores = draw_gate_scores(jax.random.fold_in(arg_keys[5], 71), 0)
    up_weight = normal_values(arg_keys[3], (EXPERTS, D, HID), D ** -0.5, 0.09375, ((0, 128), (1, 4)))
    down_weight = normal_values(arg_keys[4], (EXPERTS, HID, D), HID ** -0.5, 0.1875, ((0, 128), (2, 4)))
    return {"tokens": tokens, "route_ids": route_ids, "gate_scores": gate_scores, "up_weight": up_weight, "down_weight": down_weight}


ROUTE_SCALE = 2.5


def reference(tokens, route_ids, gate_scores, up_weight, down_weight):
    row_total = TOKENS * TOP
    flat_ids = route_ids.reshape(-1).astype(jnp.int32)
    mix_weights = gate_scores * (ROUTE_SCALE / jnp.sum(gate_scores, axis=1, keepdims=True))
    flat_weights = jnp.concatenate([mix_weights.reshape(-1), jnp.zeros((1,), jnp.float32)])
    onehot = (flat_ids[:, None] == jnp.arange(EXPERTS, dtype=jnp.int32)[None, :]).astype(jnp.int32)
    running = (jnp.cumsum(onehot, axis=0) - 1).astype(jnp.int32)
    row_ranks = jnp.sum(onehot * running, axis=1).astype(jnp.int32)
    capacity = N_EXPERT * max(HOT_MOST, COLD_MOST)
    slot_table = jnp.full((EXPERTS, capacity), row_total, jnp.int32)
    slot_table = slot_table.at[flat_ids, row_ranks].set(jnp.arange(row_total, dtype=jnp.int32))
    padded = jnp.concatenate([tokens, jnp.zeros((1, D), jnp.bfloat16)], axis=0)
    piece_width = D // N_DP

    def one_expert(totals, inputs):
        slot_rows, up_one, down_one = inputs
        token_rows = (slot_rows // TOP).astype(jnp.int32)
        gathered = padded[token_rows]
        pieces = jnp.einsum("rpc,pch->rph",
                            gathered.reshape(capacity, N_DP, piece_width).astype(jnp.float32),
                            up_one.reshape(N_DP, piece_width, HID).astype(jnp.float32))
        rounded = lax.optimization_barrier(pieces.astype(jnp.bfloat16)).astype(jnp.float32)
        before = jnp.sum(rounded, axis=1)
        hidden = jax.nn.silu(before).astype(jnp.bfloat16)
        output = jnp.dot(hidden, down_one, preferred_element_type=jnp.float32)
        output_rounded = lax.optimization_barrier(output.astype(jnp.bfloat16)).astype(jnp.float32)
        weights = flat_weights[slot_rows]
        totals = totals.at[token_rows].add(weights[:, None] * output_rounded)
        return totals, None

    start = jnp.zeros((TOKENS + 1, D), jnp.float32)
    result, unused = lax.scan(one_expert, start, (slot_table, up_weight, down_weight))
    return result[:TOKENS].astype(jnp.bfloat16)
```

```python
import jax
import jax.numpy as jnp
from jax import lax
from jax.sharding import PartitionSpec as P

HOT = 2
CHUNKS = 3


ROUTE_SCALE = 2.5


def silu_hidden(before):
    summed = lax.psum(before.astype(jnp.bfloat16), "dp").astype(jnp.float32)
    result = jax.nn.silu(summed).astype(jnp.bfloat16)
    return result


def expert_chunk(piece, up_local, down_local, previous):
    experts, item_count, features = piece.shape
    arrived = lax.all_to_all(piece, "expert", split_axis=0, concat_axis=0, tiled=True)
    flat_rows = arrived.reshape(-1, features)
    before = jnp.dot(flat_rows, up_local, preferred_element_type=jnp.float32)
    if previous is not None:
        before, previous = lax.optimization_barrier((before, previous))
    hidden = silu_hidden(before)
    output = jnp.dot(hidden, down_local, preferred_element_type=jnp.float32)
    outcome = output.astype(jnp.bfloat16).reshape(experts, item_count, features)
    returned = lax.all_to_all(outcome, "expert", split_axis=0, concat_axis=0, tiled=True)
    return returned, hidden


def local(tokens, route_ids, gate_scores, up_weight, down_weight):
    token_count, chosen_count = route_ids.shape
    features = tokens.shape[1]
    experts = lax.axis_size("expert")
    mean_rows = token_count * chosen_count // experts
    hot_most = min(2 * mean_rows - 1, token_count)
    cold_rows = (experts - HOT) * mean_rows - HOT * (hot_most - mean_rows)
    cold_most = -(-cold_rows // (experts - HOT))
    flat_ids = route_ids.reshape(-1)
    row_total = flat_ids.shape[0]
    expert_range = jnp.arange(experts, dtype=jnp.int32)
    onehot = (flat_ids[:, None] == expert_range[None, :]).astype(jnp.int32)
    running = jnp.cumsum(onehot, axis=0) - 1
    row_ranks = jnp.sum(onehot * running, axis=1)
    padded = jnp.concatenate([tokens, jnp.zeros((1, features), tokens.dtype)], axis=0)
    up_local = up_weight[0]
    down_local = down_weight[0]
    mix_weights = gate_scores * (ROUTE_SCALE / jnp.sum(gate_scores, axis=1, keepdims=True))
    slot_count = max(hot_most, cold_most)
    slot_of_row = flat_ids * slot_count + row_ranks
    slot_table = jnp.full((experts * slot_count,), row_total, jnp.int32)
    slot_table = slot_table.at[slot_of_row].set(jnp.arange(row_total, dtype=jnp.int32), mode="drop")
    sending = padded[slot_table // chosen_count].reshape(experts, slot_count, features)
    bounds = [slot_count * c // CHUNKS for c in range(CHUNKS + 1)]
    pieces = []
    previous = None
    for lo, hi in zip(bounds[:-1], bounds[1:]):
        returned, previous = expert_chunk(sending[:, lo:hi], up_local, down_local, previous)
        pieces.append(returned)
    returned = jnp.concatenate(pieces, axis=1).reshape(-1, features)
    picked = returned[slot_of_row]
    picked = picked.reshape(token_count, chosen_count, features).astype(jnp.float32)
    mixed = jnp.sum(mix_weights[:, :, None] * picked, axis=1)
    return mixed.astype(jnp.bfloat16)


def solution(mesh):
    return jax.shard_map(
        local,
        mesh=mesh,
        in_specs=(
            P("expert", "dp"),
            P("expert", None),
            P("expert", None),
            P("expert", "dp", None),
            P("expert", None, "dp"),
        ),
        out_specs=P("expert", "dp"),
        check_vma=False,
    )
```

```python
import jax
import jax.numpy as jnp
from jax import lax
from jax.sharding import PartitionSpec as P

HOT = 2
ROUTE_SCALE = 2.5
CORES = 2
Z_SIZE = 16
RELAY_OFFSETS = ((0, 0, 0), (0, 0, 1), (0, 1, 0), (0, -1, 0), (1, 0, 0), (-1, 0, 0), (0, 1, 1))


def moved(index, offset, experts, sign):
    x_size = experts // (Z_SIZE * CORES)
    x = index // (Z_SIZE * CORES)
    z = (index // CORES) % Z_SIZE
    c = index % CORES
    dx, dz, dc = offset
    x = (x + sign * dx) % x_size
    z = (z + sign * dz) % Z_SIZE
    c = (c + sign * dc) % CORES
    return (x * Z_SIZE + z) * CORES + c


def silu_hidden(before):
    summed = lax.psum(before.astype(jnp.bfloat16), "dp").astype(jnp.float32)
    result = jax.nn.silu(summed).astype(jnp.bfloat16)
    return result


def local(tokens, route_ids, gate_scores, up_weight, down_weight):
    token_count, chosen_count = route_ids.shape
    features = tokens.shape[1]
    experts = lax.axis_size("expert")
    mean_rows = token_count * chosen_count // experts
    hot_most = min(2 * mean_rows - 1, token_count)
    cold_rows = (experts - HOT) * mean_rows - HOT * (hot_most - mean_rows)
    cold_most = -(-cold_rows // (experts - HOT))
    extra = hot_most - cold_most
    relays = RELAY_OFFSETS[:extra]
    slots = cold_most + HOT
    me = lax.axis_index("expert")

    flat_ids = route_ids.reshape(-1)
    row_total = flat_ids.shape[0]
    expert_range = jnp.arange(experts, dtype=jnp.int32)
    onehot = (flat_ids[:, None] == expert_range[None, :]).astype(jnp.int32)
    running = jnp.cumsum(onehot, axis=0) - 1
    row_ranks = jnp.sum(onehot * running, axis=1)
    counts = jnp.sum(onehot, axis=0)
    _, hot_ids = lax.top_k(counts, HOT)
    hot_ids = hot_ids.astype(jnp.int32)

    is_extra = row_ranks >= cold_most
    hot_slot = jnp.argmax(flat_ids[:, None] == hot_ids[None, :], axis=1).astype(jnp.int32)
    relay_index = jnp.clip(row_ranks - cold_most, 0, extra - 1)
    relay_dest = flat_ids
    for i in range(1, extra):
        relay_dest = jnp.where(relay_index == i, moved(flat_ids, relays[i], experts, 1), relay_dest)
    dest = jnp.where(is_extra, relay_dest, flat_ids)
    slot = jnp.where(is_extra, cold_most + hot_slot, row_ranks)
    position = dest * slots + slot

    padded = jnp.concatenate([tokens, jnp.zeros((1, features), tokens.dtype)], axis=0)
    up_local = up_weight[0]
    down_local = down_weight[0]
    mix_weights = gate_scores * (ROUTE_SCALE / jnp.sum(gate_scores, axis=1, keepdims=True))
    send_table = jnp.full((experts * slots,), row_total, jnp.int32)
    send_table = send_table.at[position].set(jnp.arange(row_total, dtype=jnp.int32), mode="drop")
    sending = padded[send_table // chosen_count].reshape(experts, slots, features)
    arrived = lax.all_to_all(sending, "expert", split_axis=0, concat_axis=0, tiled=True)

    mine = jnp.where(me == hot_ids[0], 0, 1)
    own_extra = jnp.where(mine == 0, arrived[:, cold_most], arrived[:, cold_most + 1])
    hot_rows = [own_extra]
    for i in range(1, extra):
        owner = moved(me, relays[i], experts, -1)
        outgoing = jnp.where(owner == hot_ids[0], arrived[:, cold_most], arrived[:, cold_most + 1])
        pairs = [(int(moved(d, relays[i], experts, 1)), d) for d in range(experts)]
        hot_rows.append(lax.ppermute(outgoing, "expert", pairs))

    flat_rows = jnp.concatenate(
        [arrived[:, :cold_most].reshape(-1, features)] + hot_rows, axis=0
    )
    before = jnp.dot(flat_rows, up_local, preferred_element_type=jnp.float32)
    hidden = silu_hidden(before)
    output = jnp.dot(hidden, down_local, preferred_element_type=jnp.float32)
    outcome = output.astype(jnp.bfloat16)
    regular_count = experts * cold_most
    regular_out = outcome[:regular_count].reshape(experts, cold_most, features)
    hot_out = outcome[regular_count:].reshape(extra, experts, features)

    back = []
    for i in range(1, extra):
        pairs = [(d, int(moved(d, relays[i], experts, 1))) for d in range(experts)]
        back.append(lax.ppermute(hot_out[i], "expert", pairs))
    relay_out = []
    for j in range(HOT):
        result = jnp.where(me == hot_ids[j], hot_out[0], jnp.zeros_like(hot_out[0]))
        for i in range(1, extra):
            owner = moved(me, relays[i], experts, -1)
            result = jnp.where(owner == hot_ids[j], back[i - 1], result)
        relay_out.append(result[:, None])
    outgoing = jnp.concatenate([regular_out] + relay_out, axis=1)
    returned = lax.all_to_all(outgoing, "expert", split_axis=0, concat_axis=0, tiled=True)
    picked = returned.reshape(-1, features)[position]
    picked = picked.reshape(token_count, chosen_count, features).astype(jnp.float32)
    mixed = jnp.sum(mix_weights[:, :, None] * picked, axis=1)
    return mixed.astype(jnp.bfloat16)


def solution(mesh):
    return jax.shard_map(
        local,
        mesh=mesh,
        in_specs=(
            P("expert", "dp"),
            P("expert", None),
            P("expert", None),
            P("expert", "dp", None),
            P("expert", None, "dp"),
        ),
        out_specs=P("expert", "dp"),
        check_vma=False,
    )
```

```python
import jax
import jax.numpy as jnp
from jax import lax
from jax.sharding import PartitionSpec as P

HOT = 2
ROUTE_SCALE = 2.5
CORES = 2
Z_SIZE = 16
RELAY_OFFSETS = ((0, 0, 0), (0, 0, 1), (0, 1, 0), (0, -1, 0), (1, 0, 0), (-1, 0, 0), (0, 1, 1))


def moved(index, offset, experts, sign):
    x_size = experts // (Z_SIZE * CORES)
    x = index // (Z_SIZE * CORES)
    z = (index // CORES) % Z_SIZE
    c = index % CORES
    dx, dz, dc = offset
    x = (x + sign * dx) % x_size
    z = (z + sign * dz) % Z_SIZE
    c = (c + sign * dc) % CORES
    return (x * Z_SIZE + z) * CORES + c


def exchange(rows, experts):
    shape = rows.shape
    tile_rows = 8
    packed = rows.reshape(experts * tile_rows, -1)
    moved_rows = lax.all_to_all(packed, "expert", split_axis=0, concat_axis=0, tiled=True)
    return moved_rows.reshape(shape)


def silu_hidden(before):
    summed = lax.psum(before.astype(jnp.bfloat16), "dp").astype(jnp.float32)
    result = jax.nn.silu(summed).astype(jnp.bfloat16)
    return result


def local(tokens, route_ids, gate_scores, up_weight, down_weight):
    token_count, chosen_count = route_ids.shape
    features = tokens.shape[1]
    experts = lax.axis_size("expert")
    mean_rows = token_count * chosen_count // experts
    hot_most = min(2 * mean_rows - 1, token_count)
    cold_rows = (experts - HOT) * mean_rows - HOT * (hot_most - mean_rows)
    cold_most = -(-cold_rows // (experts - HOT))
    extra = hot_most - cold_most
    relays = RELAY_OFFSETS[:extra]
    slots = cold_most + HOT
    me = lax.axis_index("expert")

    flat_ids = route_ids.reshape(-1)
    row_total = flat_ids.shape[0]
    expert_range = jnp.arange(experts, dtype=jnp.int32)
    onehot = (flat_ids[:, None] == expert_range[None, :]).astype(jnp.int32)
    running = jnp.cumsum(onehot, axis=0) - 1
    row_ranks = jnp.sum(onehot * running, axis=1)
    counts = jnp.sum(onehot, axis=0)
    _, hot_ids = lax.top_k(counts, HOT)
    hot_ids = hot_ids.astype(jnp.int32)

    is_extra = row_ranks >= cold_most
    hot_slot = jnp.argmax(flat_ids[:, None] == hot_ids[None, :], axis=1).astype(jnp.int32)
    relay_index = jnp.clip(row_ranks - cold_most, 0, extra - 1)
    relay_dest = flat_ids
    for i in range(1, extra):
        relay_dest = jnp.where(relay_index == i, moved(flat_ids, relays[i], experts, 1), relay_dest)
    dest = jnp.where(is_extra, relay_dest, flat_ids)
    slot = jnp.where(is_extra, cold_most + hot_slot, row_ranks)
    position = dest * slots + slot

    padded = jnp.concatenate([tokens, jnp.zeros((1, features), tokens.dtype)], axis=0)
    up_local = up_weight[0]
    down_local = down_weight[0]
    mix_weights = gate_scores * (ROUTE_SCALE / jnp.sum(gate_scores, axis=1, keepdims=True))
    send_table = jnp.full((experts * slots,), row_total, jnp.int32)
    send_table = send_table.at[position].set(jnp.arange(row_total, dtype=jnp.int32), mode="drop")
    sending = padded[send_table // chosen_count]
    arrived = exchange(sending, experts).reshape(experts, slots, features)

    mine = jnp.where(me == hot_ids[0], 0, 1)
    own_extra = jnp.where(mine == 0, arrived[:, cold_most], arrived[:, cold_most + 1])
    hot_rows = [own_extra]
    for i in range(1, extra):
        owner = moved(me, relays[i], experts, -1)
        outgoing = jnp.where(owner == hot_ids[0], arrived[:, cold_most], arrived[:, cold_most + 1])
        pairs = [(int(moved(d, relays[i], experts, 1)), d) for d in range(experts)]
        hot_rows.append(lax.ppermute(outgoing, "expert", pairs))

    flat_rows = jnp.concatenate(
        [arrived[:, :cold_most].reshape(-1, features)] + hot_rows, axis=0
    )
    before = jnp.dot(flat_rows, up_local, preferred_element_type=jnp.float32)
    hidden = silu_hidden(before)
    output = jnp.dot(hidden, down_local, preferred_element_type=jnp.float32)
    outcome = output.astype(jnp.bfloat16)
    regular_count = experts * cold_most
    regular_out = outcome[:regular_count].reshape(experts, cold_most, features)
    hot_out = outcome[regular_count:].reshape(extra, experts, features)

    back = []
    for i in range(1, extra):
        pairs = [(d, int(moved(d, relays[i], experts, 1))) for d in range(experts)]
        back.append(lax.ppermute(hot_out[i], "expert", pairs))
    relay_out = []
    for j in range(HOT):
        result = jnp.where(me == hot_ids[j], hot_out[0], jnp.zeros_like(hot_out[0]))
        for i in range(1, extra):
            owner = moved(me, relays[i], experts, -1)
            result = jnp.where(owner == hot_ids[j], back[i - 1], result)
        relay_out.append(result[:, None])
    outgoing = jnp.concatenate([regular_out] + relay_out, axis=1)
    returned = exchange(outgoing, experts)
    picked = returned.reshape(-1, features)[position]
    picked = picked.reshape(token_count, chosen_count, features).astype(jnp.float32)
    mixed = jnp.sum(mix_weights[:, :, None] * picked, axis=1)
    return mixed.astype(jnp.bfloat16)


def solution(mesh):
    return jax.shard_map(
        local,
        mesh=mesh,
        in_specs=(
            P("expert", "dp"),
            P("expert", None),
            P("expert", None),
            P("expert", "dp", None),
            P("expert", None, "dp"),
        ),
        out_specs=P("expert", "dp"),
        check_vma=False,
    )
```

```python
import jax
import jax.numpy as jnp
from jax import lax
from jax.sharding import PartitionSpec as P

HOT = 2
ROUTE_SCALE = 2.5
CORES = 2
Z_SIZE = 16
RELAY_OFFSETS = ((0, 0, 0), (0, 0, 1), (0, 1, 0), (0, -1, 0), (1, 0, 0), (-1, 0, 0), (0, 1, 1))


def moved(index, offset, experts, sign):
    x_size = experts // (Z_SIZE * CORES)
    x = index // (Z_SIZE * CORES)
    z = (index // CORES) % Z_SIZE
    c = index % CORES
    dx, dz, dc = offset
    x = (x + sign * dx) % x_size
    z = (z + sign * dz) % Z_SIZE
    c = (c + sign * dc) % CORES
    return (x * Z_SIZE + z) * CORES + c


def exchange(rows, experts):
    shape = rows.shape
    tile_rows = 8
    packed = rows.reshape(experts * tile_rows, -1)
    moved_rows = lax.all_to_all(packed, "expert", split_axis=0, concat_axis=0, tiled=True)
    return moved_rows.reshape(shape)


def silu_hidden(befores):
    summed = lax.psum(tuple(b.astype(jnp.bfloat16) for b in befores), "dp")
    return tuple(jax.nn.silu(v.astype(jnp.float32)).astype(jnp.bfloat16) for v in summed)


def local(tokens, route_ids, gate_scores, up_weight, down_weight):
    token_count, chosen_count = route_ids.shape
    features = tokens.shape[1]
    experts = lax.axis_size("expert")
    mean_rows = token_count * chosen_count // experts
    hot_most = min(2 * mean_rows - 1, token_count)
    cold_rows = (experts - HOT) * mean_rows - HOT * (hot_most - mean_rows)
    cold_most = -(-cold_rows // (experts - HOT))
    extra = hot_most - cold_most
    relays = RELAY_OFFSETS[:extra]
    slots = cold_most + HOT
    me = lax.axis_index("expert")

    flat_ids = route_ids.reshape(-1)
    row_total = flat_ids.shape[0]
    expert_range = jnp.arange(experts, dtype=jnp.int32)
    onehot = (flat_ids[:, None] == expert_range[None, :]).astype(jnp.int32)
    running = jnp.cumsum(onehot, axis=0) - 1
    row_ranks = jnp.sum(onehot * running, axis=1)
    counts = jnp.sum(onehot, axis=0)
    _, hot_ids = lax.top_k(counts, HOT)
    hot_ids = hot_ids.astype(jnp.int32)

    is_extra = row_ranks >= cold_most
    hot_slot = jnp.argmax(flat_ids[:, None] == hot_ids[None, :], axis=1).astype(jnp.int32)
    relay_index = jnp.clip(row_ranks - cold_most, 0, extra - 1)
    relay_dest = flat_ids
    for i in range(1, extra):
        relay_dest = jnp.where(relay_index == i, moved(flat_ids, relays[i], experts, 1), relay_dest)
    dest = jnp.where(is_extra, relay_dest, flat_ids)
    slot = jnp.where(is_extra, cold_most + hot_slot, row_ranks)
    position = dest * slots + slot

    padded = jnp.concatenate([tokens, jnp.zeros((1, features), tokens.dtype)], axis=0)
    up_local = up_weight[0]
    down_local = down_weight[0]
    mix_weights = gate_scores * (ROUTE_SCALE / jnp.sum(gate_scores, axis=1, keepdims=True))
    send_table = jnp.full((experts * slots,), row_total, jnp.int32)
    send_table = send_table.at[position].set(jnp.arange(row_total, dtype=jnp.int32), mode="drop")
    sending = padded[send_table // chosen_count]
    arrived = exchange(sending, experts).reshape(experts, slots, features)

    mine = jnp.where(me == hot_ids[0], 0, 1)
    own_extra = jnp.where(mine == 0, arrived[:, cold_most], arrived[:, cold_most + 1])
    hot_rows = [own_extra]
    for i in range(1, extra):
        owner = moved(me, relays[i], experts, -1)
        outgoing = jnp.where(owner == hot_ids[0], arrived[:, cold_most], arrived[:, cold_most + 1])
        pairs = [(int(moved(d, relays[i], experts, 1)), d) for d in range(experts)]
        hot_rows.append(lax.ppermute(outgoing, "expert", pairs))

    regular_rows = arrived[:, :cold_most].reshape(-1, features)
    hot_block = jnp.stack(hot_rows).reshape(-1, features)
    regular_before = jnp.dot(regular_rows, up_local, preferred_element_type=jnp.float32)
    hot_before = jnp.dot(hot_block, up_local, preferred_element_type=jnp.float32)
    regular_hidden, hot_hidden = silu_hidden((regular_before, hot_before))
    regular_out = jnp.dot(regular_hidden, down_local, preferred_element_type=jnp.float32)
    hot_out = jnp.dot(hot_hidden, down_local, preferred_element_type=jnp.float32)
    regular_out = regular_out.astype(jnp.bfloat16).reshape(experts, cold_most, features)
    hot_out = hot_out.astype(jnp.bfloat16).reshape(extra, experts, features)

    back = []
    for i in range(1, extra):
        pairs = [(d, int(moved(d, relays[i], experts, 1))) for d in range(experts)]
        back.append(lax.ppermute(hot_out[i], "expert", pairs))
    relay_out = []
    for j in range(HOT):
        result = jnp.where(me == hot_ids[j], hot_out[0], jnp.zeros_like(hot_out[0]))
        for i in range(1, extra):
            owner = moved(me, relays[i], experts, -1)
            result = jnp.where(owner == hot_ids[j], back[i - 1], result)
        relay_out.append(result[:, None])
    outgoing = jnp.concatenate([regular_out] + relay_out, axis=1)
    returned = exchange(outgoing, experts)
    picked = returned.reshape(-1, features)[position]
    picked = picked.reshape(token_count, chosen_count, features).astype(jnp.float32)
    mixed = jnp.sum(mix_weights[:, :, None] * picked, axis=1)
    return mixed.astype(jnp.bfloat16)


def solution(mesh):
    return jax.shard_map(
        local,
        mesh=mesh,
        in_specs=(
            P("expert", "dp"),
            P("expert", None),
            P("expert", None),
            P("expert", "dp", None),
            P("expert", None, "dp"),
        ),
        out_specs=P("expert", "dp"),
        check_vma=False,
    )
```

```python
import jax
import jax.numpy as jnp
from jax import lax
from jax.sharding import PartitionSpec as P

HOT = 2
ROUTE_SCALE = 2.5
CORES = 2
Z_SIZE = 16
RELAY_OFFSETS = ((0, 0, 0), (0, 0, 1), (0, 1, 0), (0, -1, 0), (1, 0, 0), (-1, 0, 0), (0, 1, 1))


def moved(index, offset, experts, sign):
    x_size = experts // (Z_SIZE * CORES)
    x = index // (Z_SIZE * CORES)
    z = (index // CORES) % Z_SIZE
    c = index % CORES
    dx, dz, dc = offset
    x = (x + sign * dx) % x_size
    z = (z + sign * dz) % Z_SIZE
    c = (c + sign * dc) % CORES
    return (x * Z_SIZE + z) * CORES + c


def exchange(rows, experts):
    shape = rows.shape
    tile_rows = 8
    packed = rows.reshape(experts * tile_rows, -1)
    moved_rows = lax.all_to_all(packed, "expert", split_axis=0, concat_axis=0, tiled=True)
    return moved_rows.reshape(shape)


def silu_hidden(befores):
    peers = lax.axis_size("dp")
    widths = [b.shape[0] // peers for b in befores]
    blocks = jnp.concatenate(
        [b.astype(jnp.bfloat16).reshape(peers, w, b.shape[1]) for b, w in zip(befores, widths)], axis=1
    )
    parts = lax.all_to_all(blocks, "dp", 0, 0, tiled=True)
    summed = jnp.sum(parts.astype(jnp.float32), axis=0)
    hidden = jax.nn.silu(summed).astype(jnp.bfloat16)
    spread = jnp.broadcast_to(hidden[None], (peers,) + hidden.shape)
    gathered = lax.all_to_all(spread, "dp", 0, 0, tiled=True)
    results = []
    start = 0
    for b, w in zip(befores, widths):
        results.append(gathered[:, start:start + w].reshape(b.shape))
        start += w
    return tuple(results)


def local(tokens, route_ids, gate_scores, up_weight, down_weight):
    token_count, chosen_count = route_ids.shape
    features = tokens.shape[1]
    experts = lax.axis_size("expert")
    mean_rows = token_count * chosen_count // experts
    hot_most = min(2 * mean_rows - 1, token_count)
    cold_rows = (experts - HOT) * mean_rows - HOT * (hot_most - mean_rows)
    cold_most = -(-cold_rows // (experts - HOT))
    extra = hot_most - cold_most
    relays = RELAY_OFFSETS[:extra]
    slots = cold_most + HOT
    me = lax.axis_index("expert")

    flat_ids = route_ids.reshape(-1)
    row_total = flat_ids.shape[0]
    expert_range = jnp.arange(experts, dtype=jnp.int32)
    onehot = (flat_ids[:, None] == expert_range[None, :]).astype(jnp.int32)
    running = jnp.cumsum(onehot, axis=0) - 1
    row_ranks = jnp.sum(onehot * running, axis=1)
    counts = jnp.sum(onehot, axis=0)
    _, hot_ids = lax.top_k(counts, HOT)
    hot_ids = hot_ids.astype(jnp.int32)

    is_extra = row_ranks >= cold_most
    hot_slot = jnp.argmax(flat_ids[:, None] == hot_ids[None, :], axis=1).astype(jnp.int32)
    relay_index = jnp.clip(row_ranks - cold_most, 0, extra - 1)
    relay_dest = flat_ids
    for i in range(1, extra):
        relay_dest = jnp.where(relay_index == i, moved(flat_ids, relays[i], experts, 1), relay_dest)
    dest = jnp.where(is_extra, relay_dest, flat_ids)
    slot = jnp.where(is_extra, cold_most + hot_slot, row_ranks)
    position = dest * slots + slot

    padded = jnp.concatenate([tokens, jnp.zeros((1, features), tokens.dtype)], axis=0)
    up_local = up_weight[0]
    down_local = down_weight[0]
    mix_weights = gate_scores * (ROUTE_SCALE / jnp.sum(gate_scores, axis=1, keepdims=True))
    send_table = jnp.full((experts * slots,), row_total, jnp.int32)
    send_table = send_table.at[position].set(jnp.arange(row_total, dtype=jnp.int32), mode="drop")
    sending = padded[send_table // chosen_count]
    arrived = exchange(sending, experts).reshape(experts, slots, features)

    mine = jnp.where(me == hot_ids[0], 0, 1)
    own_extra = jnp.where(mine == 0, arrived[:, cold_most], arrived[:, cold_most + 1])
    hot_rows = [own_extra]
    for i in range(1, extra):
        owner = moved(me, relays[i], experts, -1)
        outgoing = jnp.where(owner == hot_ids[0], arrived[:, cold_most], arrived[:, cold_most + 1])
        pairs = [(int(moved(d, relays[i], experts, 1)), d) for d in range(experts)]
        hot_rows.append(lax.ppermute(outgoing, "expert", pairs))

    regular_rows = arrived[:, :cold_most].reshape(-1, features)
    hot_block = jnp.stack(hot_rows).reshape(-1, features)
    regular_before = jnp.dot(regular_rows, up_local, preferred_element_type=jnp.float32)
    hot_before = jnp.dot(hot_block, up_local, preferred_element_type=jnp.float32)
    regular_hidden, hot_hidden = silu_hidden((regular_before, hot_before))
    regular_out = jnp.dot(regular_hidden, down_local, preferred_element_type=jnp.float32)
    hot_out = jnp.dot(hot_hidden, down_local, preferred_element_type=jnp.float32)
    regular_out = regular_out.astype(jnp.bfloat16).reshape(experts, cold_most, features)
    hot_out = hot_out.astype(jnp.bfloat16).reshape(extra, experts, features)

    back = []
    for i in range(1, extra):
        pairs = [(d, int(moved(d, relays[i], experts, 1))) for d in range(experts)]
        back.append(lax.ppermute(hot_out[i], "expert", pairs))
    relay_out = []
    for j in range(HOT):
        result = jnp.where(me == hot_ids[j], hot_out[0], jnp.zeros_like(hot_out[0]))
        for i in range(1, extra):
            owner = moved(me, relays[i], experts, -1)
            result = jnp.where(owner == hot_ids[j], back[i - 1], result)
        relay_out.append(result[:, None])
    outgoing = jnp.concatenate([regular_out] + relay_out, axis=1)
    returned = exchange(outgoing, experts)
    picked = returned.reshape(-1, features)[position]
    picked = picked.reshape(token_count, chosen_count, features).astype(jnp.float32)
    mixed = jnp.sum(mix_weights[:, :, None] * picked, axis=1)
    return mixed.astype(jnp.bfloat16)


def solution(mesh):
    return jax.shard_map(
        local,
        mesh=mesh,
        in_specs=(
            P("expert", "dp"),
            P("expert", None),
            P("expert", None),
            P("expert", "dp", None),
            P("expert", None, "dp"),
        ),
        out_specs=P("expert", "dp"),
        check_vma=False,
    )
```

```python
import jax
import jax.numpy as jnp
from jax import lax
from jax.sharding import PartitionSpec as P

HOT = 2
ROUTE_SCALE = 2.5
CORES = 2
Z_SIZE = 16
RELAY_OFFSETS = ((0, 0, 0), (0, 0, 1), (0, 1, 0), (0, -1, 0), (1, 0, 0), (-1, 0, 0), (0, 1, 1))


def moved(index, offset, experts, sign):
    x_size = experts // (Z_SIZE * CORES)
    x = index // (Z_SIZE * CORES)
    z = (index // CORES) % Z_SIZE
    c = index % CORES
    dx, dz, dc = offset
    x = (x + sign * dx) % x_size
    z = (z + sign * dz) % Z_SIZE
    c = (c + sign * dc) % CORES
    return (x * Z_SIZE + z) * CORES + c


def exchange(rows, experts):
    shape = rows.shape
    tile_rows = 8
    packed = rows.reshape(experts * tile_rows, -1)
    moved_rows = lax.all_to_all(packed, "expert", split_axis=0, concat_axis=0, tiled=True)
    return moved_rows.reshape(shape)


def silu_hidden(befores):
    peers = lax.axis_size("dp")
    widths = [b.shape[0] // peers for b in befores]
    blocks = jnp.concatenate(
        [b.astype(jnp.bfloat16).reshape(peers, w, b.shape[1]) for b, w in zip(befores, widths)], axis=1
    )
    parts = lax.all_to_all(blocks, "dp", 0, 0, tiled=True)
    summed = jnp.sum(parts.astype(jnp.float32), axis=0)
    hidden = jax.nn.silu(summed).astype(jnp.bfloat16)
    spread = jnp.broadcast_to(hidden[None], (peers,) + hidden.shape)
    gathered = lax.all_to_all(spread, "dp", 0, 0, tiled=True)
    results = []
    start = 0
    for b, w in zip(befores, widths):
        results.append(gathered[:, start:start + w].reshape(b.shape))
        start += w
    return tuple(results)


def local(tokens, route_ids, gate_scores, up_weight, down_weight):
    token_count, chosen_count = route_ids.shape
    features = tokens.shape[1]
    experts = lax.axis_size("expert")
    mean_rows = token_count * chosen_count // experts
    hot_most = min(2 * mean_rows - 1, token_count)
    cold_rows = (experts - HOT) * mean_rows - HOT * (hot_most - mean_rows)
    cold_most = -(-cold_rows // (experts - HOT))
    extra = hot_most - cold_most
    relays = RELAY_OFFSETS[:extra]
    slots = cold_most + HOT
    me = lax.axis_index("expert")

    flat_ids = route_ids.reshape(-1)
    row_total = flat_ids.shape[0]
    expert_range = jnp.arange(experts, dtype=jnp.int32)
    onehot = (flat_ids[:, None] == expert_range[None, :]).astype(jnp.int32)
    running = jnp.cumsum(onehot, axis=0) - 1
    row_ranks = jnp.sum(onehot * running, axis=1)
    counts = jnp.sum(onehot, axis=0)
    _, hot_ids = lax.top_k(counts, HOT)
    hot_ids = hot_ids.astype(jnp.int32)

    is_extra = row_ranks >= cold_most
    hot_slot = jnp.argmax(flat_ids[:, None] == hot_ids[None, :], axis=1).astype(jnp.int32)
    relay_index = jnp.clip(row_ranks - cold_most, 0, extra - 1)
    relay_dest = flat_ids
    for i in range(1, extra):
        relay_dest = jnp.where(relay_index == i, moved(flat_ids, relays[i], experts, 1), relay_dest)
    dest = jnp.where(is_extra, relay_dest, flat_ids)
    slot = jnp.where(is_extra, cold_most + hot_slot, row_ranks)
    position = dest * slots + slot

    padded = jnp.concatenate([tokens, jnp.zeros((1, features), tokens.dtype)], axis=0)
    up_local = up_weight[0]
    down_local = down_weight[0]
    mix_weights = gate_scores * (ROUTE_SCALE / jnp.sum(gate_scores, axis=1, keepdims=True))
    send_table = jnp.full((experts * slots,), row_total, jnp.int32)
    send_table = send_table.at[position].set(jnp.arange(row_total, dtype=jnp.int32), mode="drop")
    sending = padded[send_table // chosen_count]
    arrived = exchange(sending, experts).reshape(experts, slots, features)

    mine = jnp.where(me == hot_ids[0], 0, 1)
    own_extra = jnp.where(mine == 0, arrived[:, cold_most], arrived[:, cold_most + 1])
    hot_rows = [own_extra]
    for i in range(1, extra):
        owner = moved(me, relays[i], experts, -1)
        outgoing = jnp.where(owner == hot_ids[0], arrived[:, cold_most], arrived[:, cold_most + 1])
        pairs = [(int(moved(d, relays[i], experts, 1)), d) for d in range(experts)]
        hot_rows.append(lax.ppermute(outgoing, "expert", pairs))

    regular_rows = arrived[:, :cold_most].reshape(-1, features)
    hot_block = jnp.stack(hot_rows).reshape(-1, features)
    regular_before = jnp.dot(regular_rows, up_local, preferred_element_type=jnp.float32)
    hot_before = jnp.dot(hot_block, up_local, preferred_element_type=jnp.float32)
    regular_hidden, hot_hidden = silu_hidden((regular_before, hot_before))
    regular_out = jnp.dot(regular_hidden, down_local, preferred_element_type=jnp.float32)
    hot_out = jnp.dot(hot_hidden, down_local, preferred_element_type=jnp.float32)
    regular_out = regular_out.astype(jnp.bfloat16).reshape(experts, cold_most, features)
    hot_out = hot_out.astype(jnp.bfloat16).reshape(extra, experts, features)

    back = []
    for i in range(1, extra):
        pairs = [(d, int(moved(d, relays[i], experts, 1))) for d in range(experts)]
        back.append(lax.ppermute(hot_out[i], "expert", pairs))
    relay_out = []
    for j in range(HOT):
        result = jnp.where(me == hot_ids[j], hot_out[0], jnp.zeros_like(hot_out[0]))
        for i in range(1, extra):
            owner = moved(me, relays[i], experts, -1)
            result = jnp.where(owner == hot_ids[j], back[i - 1], result)
        relay_out.append(result[:, None])
    outgoing = jnp.concatenate([regular_out] + relay_out, axis=1)
    returned = exchange(outgoing, experts)
    slot_range = jnp.arange(experts * slots, dtype=jnp.int32)
    chosen_at = position.reshape(token_count, chosen_count)[:, :, None] == slot_range[None, None, :]
    mixing = jnp.sum(jnp.where(chosen_at, mix_weights[:, :, None], 0.0), axis=1)
    mixed = jnp.dot(
        mixing,
        returned.reshape(-1, features).astype(jnp.float32),
        precision=lax.Precision.HIGHEST,
        preferred_element_type=jnp.float32,
    )
    return mixed.astype(jnp.bfloat16)


def solution(mesh):
    return jax.shard_map(
        local,
        mesh=mesh,
        in_specs=(
            P("expert", "dp"),
            P("expert", None),
            P("expert", None),
            P("expert", "dp", None),
            P("expert", None, "dp"),
        ),
        out_specs=P("expert", "dp"),
        check_vma=False,
    )
```

```python
import jax
import jax.numpy as jnp
from jax import lax
from jax.sharding import PartitionSpec as P

HOT = 2
ROUTE_SCALE = 2.5
CORES = 2
Z_SIZE = 16
RELAY_OFFSETS = ((0, 0, 0), (0, 0, 1), (0, 1, 0), (0, -1, 0), (1, 0, 0), (-1, 0, 0), (0, 1, 1))


def moved(index, offset, experts, sign):
    x_size = experts // (Z_SIZE * CORES)
    x = index // (Z_SIZE * CORES)
    z = (index // CORES) % Z_SIZE
    c = index % CORES
    dx, dz, dc = offset
    x = (x + sign * dx) % x_size
    z = (z + sign * dz) % Z_SIZE
    c = (c + sign * dc) % CORES
    return (x * Z_SIZE + z) * CORES + c


def exchange(rows, experts):
    shape = rows.shape
    tile_rows = 8
    packed = rows.reshape(experts * tile_rows, -1)
    moved_rows = lax.all_to_all(packed, "expert", split_axis=0, concat_axis=0, tiled=True)
    return moved_rows.reshape(shape)


def silu_hidden(befores):
    peers = lax.axis_size("dp")
    widths = [b.shape[0] // peers for b in befores]
    blocks = jnp.concatenate(
        [b.astype(jnp.bfloat16).reshape(peers, w, b.shape[1]) for b, w in zip(befores, widths)], axis=1
    )
    parts = lax.all_to_all(blocks, "dp", 0, 0, tiled=True)
    summed = jnp.sum(parts.astype(jnp.float32), axis=0)
    hidden = jax.nn.silu(summed).astype(jnp.bfloat16)
    spread = jnp.broadcast_to(hidden[None], (peers,) + hidden.shape)
    gathered = lax.all_to_all(spread, "dp", 0, 0, tiled=True)
    results = []
    start = 0
    for b, w in zip(befores, widths):
        results.append(gathered[:, start:start + w].reshape(b.shape))
        start += w
    return tuple(results)


def local(tokens, route_ids, gate_scores, up_weight, down_weight):
    token_count, chosen_count = route_ids.shape
    features = tokens.shape[1]
    experts = lax.axis_size("expert")
    mean_rows = token_count * chosen_count // experts
    hot_most = min(2 * mean_rows - 1, token_count)
    cold_rows = (experts - HOT) * mean_rows - HOT * (hot_most - mean_rows)
    cold_most = -(-cold_rows // (experts - HOT))
    extra = hot_most - cold_most
    relays = RELAY_OFFSETS[:extra]
    slots = cold_most + HOT
    me = lax.axis_index("expert")

    flat_ids = route_ids.reshape(-1)
    row_total = flat_ids.shape[0]
    expert_range = jnp.arange(experts, dtype=jnp.int32)
    onehot = (flat_ids[:, None] == expert_range[None, :]).astype(jnp.int32)
    running = jnp.cumsum(onehot, axis=0) - 1
    row_ranks = jnp.sum(onehot * running, axis=1)
    counts = jnp.sum(onehot, axis=0)
    _, hot_ids = lax.top_k(counts, HOT)
    hot_ids = hot_ids.astype(jnp.int32)

    is_extra = row_ranks >= cold_most
    hot_slot = jnp.argmax(flat_ids[:, None] == hot_ids[None, :], axis=1).astype(jnp.int32)
    relay_index = jnp.clip(row_ranks - cold_most, 0, extra - 1)
    relay_dest = flat_ids
    for i in range(1, extra):
        relay_dest = jnp.where(relay_index == i, moved(flat_ids, relays[i], experts, 1), relay_dest)
    dest = jnp.where(is_extra, relay_dest, flat_ids)
    slot = jnp.where(is_extra, cold_most + hot_slot, row_ranks)
    position = dest * slots + slot

    padded = jnp.concatenate([tokens, jnp.zeros((1, features), tokens.dtype)], axis=0)
    up_local = up_weight[0]
    down_local = down_weight[0]
    mix_weights = gate_scores * (ROUTE_SCALE / jnp.sum(gate_scores, axis=1, keepdims=True))
    send_table = jnp.full((experts * slots,), row_total, jnp.int32)
    send_table = send_table.at[position].set(jnp.arange(row_total, dtype=jnp.int32), mode="drop")
    token_range = jnp.arange(token_count, dtype=jnp.int32)
    picks = ((send_table // chosen_count)[:, None] == token_range[None, :]).astype(tokens.dtype)
    sending = jnp.dot(picks, tokens, preferred_element_type=jnp.float32).astype(tokens.dtype)
    arrived = exchange(sending, experts).reshape(experts, slots, features)

    mine = jnp.where(me == hot_ids[0], 0, 1)
    own_extra = jnp.where(mine == 0, arrived[:, cold_most], arrived[:, cold_most + 1])
    hot_rows = [own_extra]
    for i in range(1, extra):
        owner = moved(me, relays[i], experts, -1)
        outgoing = jnp.where(owner == hot_ids[0], arrived[:, cold_most], arrived[:, cold_most + 1])
        pairs = [(int(moved(d, relays[i], experts, 1)), d) for d in range(experts)]
        hot_rows.append(lax.ppermute(outgoing, "expert", pairs))

    regular_rows = arrived[:, :cold_most].reshape(-1, features)
    hot_block = jnp.stack(hot_rows).reshape(-1, features)
    regular_before = jnp.dot(regular_rows, up_local, preferred_element_type=jnp.float32)
    hot_before = jnp.dot(hot_block, up_local, preferred_element_type=jnp.float32)
    regular_hidden, hot_hidden = silu_hidden((regular_before, hot_before))
    regular_out = jnp.dot(regular_hidden, down_local, preferred_element_type=jnp.float32)
    hot_out = jnp.dot(hot_hidden, down_local, preferred_element_type=jnp.float32)
    regular_out = regular_out.astype(jnp.bfloat16).reshape(experts, cold_most, features)
    hot_out = hot_out.astype(jnp.bfloat16).reshape(extra, experts, features)

    back = []
    for i in range(1, extra):
        pairs = [(d, int(moved(d, relays[i], experts, 1))) for d in range(experts)]
        back.append(lax.ppermute(hot_out[i], "expert", pairs))
    relay_out = []
    for j in range(HOT):
        result = jnp.where(me == hot_ids[j], hot_out[0], jnp.zeros_like(hot_out[0]))
        for i in range(1, extra):
            owner = moved(me, relays[i], experts, -1)
            result = jnp.where(owner == hot_ids[j], back[i - 1], result)
        relay_out.append(result[:, None])
    outgoing = jnp.concatenate([regular_out] + relay_out, axis=1)
    returned = exchange(outgoing, experts)
    slot_range = jnp.arange(experts * slots, dtype=jnp.int32)
    chosen_at = position.reshape(token_count, chosen_count)[:, :, None] == slot_range[None, None, :]
    mixing = jnp.sum(jnp.where(chosen_at, mix_weights[:, :, None], 0.0), axis=1)
    mixed = jnp.dot(
        mixing,
        returned.reshape(-1, features).astype(jnp.float32),
        precision=lax.Precision.HIGHEST,
        preferred_element_type=jnp.float32,
    )
    return mixed.astype(jnp.bfloat16)


def solution(mesh):
    return jax.shard_map(
        local,
        mesh=mesh,
        in_specs=(
            P("expert", "dp"),
            P("expert", None),
            P("expert", None),
            P("expert", "dp", None),
            P("expert", None, "dp"),
        ),
        out_specs=P("expert", "dp"),
        check_vma=False,
    )
```

```python
import jax
import jax.numpy as jnp
from jax import lax
from jax.sharding import PartitionSpec as P

HOT = 2
ROUTE_SCALE = 2.5
CORES = 2
Z_SIZE = 16
RELAY_OFFSETS = ((0, 0, 0), (0, 0, 1), (0, 1, 0), (0, -1, 0), (1, 0, 0), (-1, 0, 0), (0, 1, 1))


def moved(index, offset, experts, sign):
    x_size = experts // (Z_SIZE * CORES)
    x = index // (Z_SIZE * CORES)
    z = (index // CORES) % Z_SIZE
    c = index % CORES
    dx, dz, dc = offset
    x = (x + sign * dx) % x_size
    z = (z + sign * dz) % Z_SIZE
    c = (c + sign * dc) % CORES
    return (x * Z_SIZE + z) * CORES + c


def exchange(rows, experts):
    shape = rows.shape
    tile_rows = 8
    packed = rows.reshape(experts * tile_rows, -1)
    moved_rows = lax.all_to_all(packed, "expert", split_axis=0, concat_axis=0, tiled=True)
    return moved_rows.reshape(shape)


def silu_hidden(befores):
    peers = lax.axis_size("dp")
    widths = [b.shape[0] // peers for b in befores]
    blocks = jnp.concatenate(
        [b.astype(jnp.bfloat16).reshape(peers, w, b.shape[1]) for b, w in zip(befores, widths)], axis=1
    )
    parts = lax.all_to_all(blocks, "dp", 0, 0, tiled=True)
    summed = jnp.sum(parts.astype(jnp.float32), axis=0)
    hidden = jax.nn.silu(summed).astype(jnp.bfloat16)
    spread = jnp.broadcast_to(hidden[None], (peers,) + hidden.shape)
    gathered = lax.all_to_all(spread, "dp", 0, 0, tiled=True)
    results = []
    start = 0
    for b, w in zip(befores, widths):
        results.append(gathered[:, start:start + w].reshape(b.shape))
        start += w
    return tuple(results)


def local(tokens, route_ids, gate_scores, up_weight, down_weight):
    token_count, chosen_count = route_ids.shape
    features = tokens.shape[1]
    experts = lax.axis_size("expert")
    mean_rows = token_count * chosen_count // experts
    hot_most = min(2 * mean_rows - 1, token_count)
    cold_rows = (experts - HOT) * mean_rows - HOT * (hot_most - mean_rows)
    cold_most = -(-cold_rows // (experts - HOT))
    extra = hot_most - cold_most
    relays = RELAY_OFFSETS[:extra]
    slots = cold_most + HOT
    me = lax.axis_index("expert")

    flat_ids = route_ids.reshape(-1)
    row_total = flat_ids.shape[0]
    expert_range = jnp.arange(experts, dtype=jnp.int32)
    onehot = (flat_ids[:, None] == expert_range[None, :]).astype(jnp.int32)
    running = jnp.cumsum(onehot, axis=0) - 1
    row_ranks = jnp.sum(onehot * running, axis=1)
    counts = jnp.sum(onehot, axis=0)
    _, hot_ids = lax.top_k(counts, HOT)
    hot_ids = hot_ids.astype(jnp.int32)

    is_extra = row_ranks >= cold_most
    hot_slot = jnp.argmax(flat_ids[:, None] == hot_ids[None, :], axis=1).astype(jnp.int32)
    relay_index = jnp.clip(row_ranks - cold_most, 0, extra - 1)
    relay_dest = flat_ids
    for i in range(1, extra):
        relay_dest = jnp.where(relay_index == i, moved(flat_ids, relays[i], experts, 1), relay_dest)
    dest = jnp.where(is_extra, relay_dest, flat_ids)
    slot = jnp.where(is_extra, cold_most + hot_slot, row_ranks)
    position = dest * slots + slot

    padded = jnp.concatenate([tokens, jnp.zeros((1, features), tokens.dtype)], axis=0)
    up_local = up_weight[0]
    down_local = down_weight[0]
    mix_weights = gate_scores * (ROUTE_SCALE / jnp.sum(gate_scores, axis=1, keepdims=True))
    send_table = jnp.full((experts * slots,), row_total, jnp.int32)
    send_table = send_table.at[position].set(jnp.arange(row_total, dtype=jnp.int32), mode="drop")
    token_range = jnp.arange(token_count, dtype=jnp.int32)
    picks = ((send_table // chosen_count)[:, None] == token_range[None, :]).astype(tokens.dtype)
    sending = jnp.dot(picks, tokens, preferred_element_type=jnp.float32).astype(tokens.dtype)
    arrived = exchange(sending, experts).reshape(experts, slots, features)

    mine = jnp.where(me == hot_ids[0], 0, 1)
    own_extra = lax.dynamic_index_in_dim(arrived, cold_most + mine, axis=1, keepdims=False)
    hot_rows = [own_extra]
    for i in range(1, extra):
        owner = moved(me, relays[i], experts, -1)
        outgoing = jnp.where(owner == hot_ids[0], arrived[:, cold_most], arrived[:, cold_most + 1])
        pairs = [(int(moved(d, relays[i], experts, 1)), d) for d in range(experts)]
        hot_rows.append(lax.ppermute(outgoing, "expert", pairs))

    regular_rows = arrived[:, :cold_most].reshape(-1, features)
    hot_block = jnp.stack(hot_rows).reshape(-1, features)
    regular_before = jnp.dot(regular_rows, up_local, preferred_element_type=jnp.float32)
    hot_before = jnp.dot(hot_block, up_local, preferred_element_type=jnp.float32)
    regular_hidden, hot_hidden = silu_hidden((regular_before, hot_before))
    regular_out = jnp.dot(regular_hidden, down_local, preferred_element_type=jnp.float32)
    hot_out = jnp.dot(hot_hidden, down_local, preferred_element_type=jnp.float32)
    regular_out = regular_out.astype(jnp.bfloat16).reshape(experts, cold_most, features)
    hot_out = hot_out.astype(jnp.bfloat16).reshape(extra, experts, features)

    back = []
    for i in range(1, extra):
        pairs = [(d, int(moved(d, relays[i], experts, 1))) for d in range(experts)]
        back.append(lax.ppermute(hot_out[i], "expert", pairs))
    relay_out = []
    for j in range(HOT):
        result = jnp.where(me == hot_ids[j], hot_out[0], jnp.zeros_like(hot_out[0]))
        for i in range(1, extra):
            owner = moved(me, relays[i], experts, -1)
            result = jnp.where(owner == hot_ids[j], back[i - 1], result)
        relay_out.append(result[:, None])
    outgoing = jnp.concatenate([regular_out] + relay_out, axis=1)
    returned = exchange(outgoing, experts)
    slot_range = jnp.arange(experts * slots, dtype=jnp.int32)
    chosen_at = position.reshape(token_count, chosen_count)[:, :, None] == slot_range[None, None, :]
    mixing = jnp.sum(jnp.where(chosen_at, mix_weights[:, :, None], 0.0), axis=1)
    mixed = jnp.dot(
        mixing,
        returned.reshape(-1, features).astype(jnp.float32),
        precision=lax.Precision.HIGHEST,
        preferred_element_type=jnp.float32,
    )
    return mixed.astype(jnp.bfloat16)


def solution(mesh):
    return jax.shard_map(
        local,
        mesh=mesh,
        in_specs=(
            P("expert", "dp"),
            P("expert", None),
            P("expert", None),
            P("expert", "dp", None),
            P("expert", None, "dp"),
        ),
        out_specs=P("expert", "dp"),
        check_vma=False,
    )
```
